32 devices in a mesh: dp: 8 (over z, x), tensor: 4 (over y, core).
Axes of the slice: x: 2, y: 2, z: 4, core: 2. Of those that a mesh axis runs over, the one named last changes fastest.
Arguments:
- hidden: bfloat16 [16384, 1024], P('dp'), may hold values from -6 to 6
- lengths: int32 [8], P('dp'), may hold values from 1365 to 2048, as said below
- norm_gain: float32 [1024], replicated, may hold values from 0.1 to 1.9
- z_weight: bfloat16 [1024, 2048], P(None, 'tensor'), may hold values from -0.1875 to 0.1875
- x_weight: bfloat16 [1024, 2048], P(None, 'tensor'), may hold values from -0.1875 to 0.1875
- bc_weight: bfloat16 [1024, 256], replicated, may hold values from -0.1875 to 0.1875
- dt_weight: bfloat16 [1024, 32], P(None, 'tensor'), may hold values from -0.1875 to 0.1875
- x_kernel: float32 [4, 2048], P(None, 'tensor'), may hold values from -3 to 3
- bc_kernel: float32 [4, 256], replicated, may hold values from -3 to 3
- x_offset: float32 [2048], P('tensor'), may hold values from -3 to 3
- bc_offset: float32 [256], replicated, may hold values from -3 to 3
- step_bias: float32 [32], P('tensor'), may hold values from -5 to -1
- decay_log: float32 [32], P('tensor'), may hold values from 0 to 2.5
- skip_gain: float32 [32], P('tensor'), may hold values from 0.5 to 1.5
- gate_gain: float32 [2048], P('tensor'), may hold values from 0.1 to 1.9
- out_weight: bfloat16 [2048, 1024], P('tensor'), may hold values from -0.125 to 0.125
- cotangent: bfloat16 [16384, 1024], P('dp'), may hold values from -6 to 6
Outputs:
- output: bfloat16 [16384, 1024], P('dp')
- grad_hidden: float32 [16384, 1024], P('dp')
- grad_norm_gain: float32 [1024], replicated
- grad_z_weight: float32 [1024, 2048], P(None, 'tensor')
- grad_x_weight: float32 [1024, 2048], P(None, 'tensor')
- grad_bc_weight: float32 [1024, 256], replicated
- grad_dt_weight: float32 [1024, 32], P(None, 'tensor')
- grad_x_kernel: float32 [4, 2048], P(None, 'tensor')
- grad_bc_kernel: float32 [4, 256], replicated
- grad_x_offset: float32 [2048], P('tensor')
- grad_bc_offset: float32 [256], replicated
- grad_step_bias: float32 [32], P('tensor')
- grad_decay_log: float32 [32], P('tensor')
- grad_skip_gain: float32 [32], P('tensor')
- grad_gate_gain: float32 [2048], P('tensor')
- grad_out_weight: float32 [2048, 1024], P('tensor')
The draws below stay inside these ranges and needn't reach their ends.
Inputs may be any that keep to these rules, and one draw needn't show every extreme that they name: `lengths`: each slot's sequence length; some slot has exactly 2048 in every draw.
All inputs are finite; a program needn't handle non-finite values.
Results may differ from the reference program's by a relative error of at most 0.0096.
Values may be sent and summed in bfloat16 or wider, within the bound.
No kernel may reach another device: no remote copies, remote signals or barrier semaphores. Data moves between devices by JAX's collectives and lax.ppermute only.
A program may use at most 192 MiB of HBM per device.

```python
import jax
import jax.numpy as jnp
from jax import lax

D = 1024
H = 32
NS = 128
KC = 4
CH = 256
SLOT = 2048
LEN_LO = 1365
SLOTS = 8
TOKENS = 16384
DI = 2048


def draw_lengths(key, part):
    first_key, second_key = jax.random.split(jax.random.fold_in(key, 17))
    drawn = jax.random.randint(first_key, (SLOTS,), LEN_LO, SLOT + 1)
    full_slot = jax.random.randint(second_key, (), 0, SLOTS)
    return jnp.where(lax.iota(jnp.int32, SLOTS) == full_slot, SLOT, drawn).astype(jnp.int32)


def level_of(stream_key, dims, pieces, low, high):
    factor_of, own = 1.0, jax.random.fold_in(stream_key, 6)
    for dim, blocks in pieces:
        heights = jnp.exp(jax.random.uniform(jax.random.fold_in(own, dim), (blocks,), jnp.float32, low / len(pieces), high / len(pieces)))
        factor_of = factor_of * jnp.repeat(heights, dims[dim] // blocks).reshape([-1 if axis == dim else 1 for axis in range(len(dims))])
    return factor_of


def scatter_about(rng, shape, deviation, limit, cuts=(), kind=jnp.bfloat16):
    array = jax.random.normal(rng, shape, jnp.float32) * deviation
    if len(cuts) > 0:
        array = level_of(rng, shape, cuts, -0.22, 0.18) * array
    return jnp.clip(array, min=-limit, max=limit).astype(kind)


def setup_inputs(seed: int = 0) -> dict:
    arg_keys = jax.random.split(jax.random.key(seed), 18)
    hidden = scatter_about(arg_keys[0], (TOKENS, D), 1.0, 6.0, ((0, 8),))
    lengths = draw_lengths(jax.random.fold_in(arg_keys[17], 71), 0)
    norm_gain = jnp.clip(1.0 + 0.18 * jax.random.normal(arg_keys[2], (D,), jnp.float32), 0.1, 1.9)
    z_weight = scatter_about(arg_keys[3], (D, DI), D ** -0.5, 0.1875, ((1, 4),))
    x_weight = scatter_about(arg_keys[4], (D, DI), D ** -0.5, 0.1875, ((1, 4),))
    bc_weight = scatter_about(arg_keys[5], (D, 2 * NS), D ** -0.5, 0.1875)
    dt_weight = scatter_about(arg_keys[6], (D, H), D ** -0.5, 0.1875, ((1, 4),))
    x_kernel = scatter_about(arg_keys[7], (KC, DI), 0.5, 3.0, ((1, 4),), jnp.float32)
    bc_kernel = scatter_about(arg_keys[8], (KC, 2 * NS), 0.5, 3.0, (), jnp.float32)
    x_offset = scatter_about(arg_keys[9], (DI,), 0.5, 3.0, ((0, 4),), jnp.float32)
    bc_offset = scatter_about(arg_keys[10], (2 * NS,), 0.5, 3.0, (), jnp.float32)
    step_bias = jnp.clip(-5.0 + 4.0 * jax.random.uniform(arg_keys[11], (H,), jnp.float32) ** level_of(arg_keys[11], (H,), ((0, 4),), -0.2, 0.2), -5.0, -1.0)
    decay_log = jnp.clip(2.5 * jax.random.uniform(arg_keys[12], (H,), jnp.float32) ** level_of(arg_keys[12], (H,), ((0, 4),), -0.2, 0.2), 0.0, 2.5)
    skip_gain = jnp.clip(0.5 + 1.0 * jax.random.uniform(arg_keys[13], (H,), jnp.float32) ** level_of(arg_keys[13], (H,), ((0, 4),), -0.2, 0.2), 0.5, 1.5)
    gate_gain = jnp.clip(1.0 + 0.18 * jax.random.normal(arg_keys[14], (DI,), jnp.float32), 0.1, 1.9)
    out_weight = scatter_about(arg_keys[15], (DI, D), DI ** -0.5, 0.125, ((0, 4),))
    cotangent = scatter_about(arg_keys[16], (TOKENS, D), 1.0, 6.0, ((0, 8),))
    return {"hidden": hidden, "lengths": lengths, "norm_gain": norm_gain, "z_weight": z_weight, "x_weight": x_weight, "bc_weight": bc_weight, "dt_weight": dt_weight, "x_kernel": x_kernel, "bc_kernel": bc_kernel, "x_offset": x_offset, "bc_offset": bc_offset, "step_bias": step_bias, "decay_log": decay_log, "skip_gain": skip_gain, "gate_gain": gate_gain, "out_weight": out_weight, "cotangent": cotangent}


@jax.custom_vjp
def low(v):
    return lax.optimization_barrier(v.astype(jnp.bfloat16)).astype(jnp.float32)

@jax.custom_vjp
def low_back(v):
    return v

def low_keep(v):
    return (low(v), None)

def low_pass(kept, grad):
    return (grad,)

def back_keep(v):
    return (v, None)

def back_low(kept, grad):
    return (low(grad),)
low.defvjp(low_keep, low_pass)
low_back.defvjp(back_keep, back_low)
precise = lax.Precision.HIGHEST
epsilon = 1e-05

def matmul(left, right):
    return jnp.dot(left, right, precision=precise, preferred_element_type=jnp.float32)

def causal_conv(signal, kernel, offset):
    taps = kernel.shape[0]
    length = signal.shape[0]
    padded = jnp.pad(signal, ((taps - 1, 0), (0, 0)))
    total = jnp.zeros_like(signal) + offset[None, :]
    for tap_index in range(taps):
        total = total + kernel[tap_index][None, :] * padded[tap_index:tap_index + length]
    return total

def conv_act(signal, kernel, offset):
    return jax.nn.silu(causal_conv(signal, kernel, offset))

def group_step(carry_state, block_in):
    values, log_rates, b_rows, c_rows = block_in
    block_len = log_rates.shape[1]
    causal_mask = lax.broadcasted_iota(jnp.int32, (block_len, block_len), 0) >= lax.broadcasted_iota(jnp.int32, (block_len, block_len), 1)
    summed = jnp.cumsum(log_rates, axis=1)
    spread = summed[:, :, None] - summed[:, None, :]
    decays = jnp.exp(jnp.where(causal_mask[None], spread, -1e+30))
    scores = jnp.dot(c_rows, b_rows.T, precision=precise, preferred_element_type=jnp.float32)
    within = jnp.einsum('hts,hsp->htp', scores[None] * decays, values, precision=precise)
    carried = jnp.einsum('tn,hnp->htp', c_rows, carry_state, precision=precise) * jnp.exp(summed)[:, :, None]
    remain = jnp.exp(summed[:, -1:] - summed)
    updated = carry_state * jnp.exp(summed[:, -1])[:, None, None] + jnp.einsum('sn,hsp->hnp', b_rows, values * remain[:, :, None], precision=precise)
    return (updated, within + carried)

def mixer(conv_vals, state_vals, step_raw, step_bias, decay_log, skip_gain, live_mask):
    row_count, channels = conv_vals.shape
    head_count = step_raw.shape[1]
    head_size = channels // head_count
    state_size = state_vals.shape[1] // 2
    block_count = row_count // CH
    step_size = jax.nn.softplus(step_raw + step_bias[None, :]) * live_mask[:, None]
    log_rates = step_size * (-jnp.exp(decay_log))[None, :]
    heads_view = conv_vals.reshape(row_count, head_count, head_size)
    values = heads_view * step_size[:, :, None]
    values = values.reshape(block_count, CH, head_count, head_size).transpose(0, 2, 1, 3)
    log_rates = log_rates.reshape(block_count, CH, head_count).transpose(0, 2, 1)
    b_rows = state_vals[:, :state_size].reshape(block_count, CH, state_size)
    c_rows = state_vals[:, state_size:].reshape(block_count, CH, state_size)
    start_state = jnp.zeros((head_count, state_size, head_size), jnp.float32)
    unused, results = lax.scan(jax.checkpoint(group_step), start_state, (values, log_rates, b_rows, c_rows))
    mixed = results.transpose(0, 2, 1, 3).reshape(row_count, head_count, head_size)
    mixed = mixed + skip_gain[None, :, None] * heads_view
    return mixed.reshape(row_count, channels)

def forward_slot(weights, slot_in, seq_len):
    norm_gain, z_weight, x_weight, bc_weight, dt_weight, x_kernel, bc_kernel, x_offset, bc_offset, step_bias, decay_log, skip_gain, gate_gain, out_weight = weights
    live_mask = (lax.iota(jnp.int32, SLOT) < seq_len).astype(jnp.float32)
    scale = lax.rsqrt(lax.optimization_barrier(jnp.mean(slot_in * slot_in, axis=1, keepdims=True)) + epsilon)
    normed = low(slot_in * scale * norm_gain[None, :])
    gate_pre = low_back(matmul(normed, z_weight))
    conv_in = low_back(matmul(normed, x_weight))
    state_in = low_back(matmul(normed, bc_weight))
    step_raw = low_back(matmul(normed, dt_weight))
    conv_low = low(conv_act(conv_in, x_kernel, x_offset))
    state_low = low(conv_act(state_in, bc_kernel, bc_offset))
    mixed_out = mixer(conv_low, state_low, step_raw, step_bias, decay_log, skip_gain, live_mask)
    gated = mixed_out * jax.nn.silu(gate_pre)
    inv_norm = lax.rsqrt(lax.optimization_barrier(jnp.mean(gated * gated, axis=1, keepdims=True)) + epsilon)
    branch_in = low(gated * inv_norm * gate_gain[None, :] * live_mask[:, None])
    return slot_in + matmul(branch_in, out_weight)

def reference(hidden, lengths, norm_gain, z_weight, x_weight, bc_weight, dt_weight, x_kernel, bc_kernel, x_offset, bc_offset, step_bias, decay_log, skip_gain, gate_gain, out_weight, cotangent):
    weights = tuple((item.astype(jnp.float32) for item in (norm_gain, z_weight, x_weight, bc_weight, dt_weight, x_kernel, bc_kernel, x_offset, bc_offset, step_bias, decay_log, skip_gain, gate_gain, out_weight)))

    def one_slot(totals, slot_data):
        slot_in, seq_len, slot_grad = slot_data
        result, pull = jax.vjp(lambda inner, params: forward_slot(params, inner, seq_len), slot_in, weights)
        grad_in, grad_params = pull(slot_grad)
        return (jax.tree.map(jnp.add, totals, grad_params), (result.astype(jnp.bfloat16), grad_in))
    zeros = jax.tree.map(jnp.zeros_like, weights)
    slots_in = hidden.reshape(SLOTS, SLOT, D).astype(jnp.float32)
    slots_grad = cotangent.reshape(SLOTS, SLOT, D).astype(jnp.float32)
    totals, (outputs, grads) = lax.scan(one_slot, zeros, (slots_in, lengths, slots_grad))
    return (outputs.reshape(TOKENS, D), grads.reshape(TOKENS, D), totals[0], totals[1], totals[2], totals[3], totals[4], totals[5], totals[6], totals[7], totals[8], totals[9], totals[10], totals[11], totals[12], totals[13])
```

```python
import jax
import jax.numpy as jnp
from jax import lax
from jax.sharding import PartitionSpec as P

CH = 256
DI = 2048


precise = lax.Precision.HIGHEST
epsilon = 1e-05


def causal_conv(signal, kernel, offset):
    taps = kernel.shape[0]
    length = signal.shape[0]
    padded = jnp.pad(signal, ((taps - 1, 0), (0, 0)))
    total = jnp.zeros_like(signal) + offset[None, :]
    for tap_index in range(taps):
        total = total + kernel[tap_index][None, :] * padded[tap_index : tap_index + length]
    return total


def conv_act(signal, kernel, offset):
    return jax.nn.silu(causal_conv(signal, kernel, offset))


def mixer(conv_vals, state_vals, step_raw, step_bias, decay_log, skip_gain, live_mask):
    R, channels = conv_vals.shape
    h = step_raw.shape[1]
    p = channels // h
    n = state_vals.shape[1] // 2
    nb = R // CH
    step_size = jax.nn.softplus(step_raw + step_bias[None, :]) * live_mask[:, None]
    log_rates = step_size * (-jnp.exp(decay_log))[None, :]
    heads_view = conv_vals.reshape(R, h, p)
    vals = (heads_view * step_size[:, :, None]).reshape(nb, CH, h, p)
    lr = log_rates.reshape(nb, CH, h)
    B = state_vals[:, :n].reshape(nb, CH, n)
    C = state_vals[:, n:].reshape(nb, CH, n)
    tri = (lax.broadcasted_iota(jnp.int32, (CH, CH), 0) >= lax.broadcasted_iota(jnp.int32, (CH, CH), 1))
    summed = jnp.einsum('ts,bsh->bth', tri.astype(jnp.float32), lr, precision=precise)
    spread = summed[:, :, None, :] - summed[:, None, :, :]
    decays = jnp.exp(jnp.where(tri[None, :, :, None], spread, -1e30))
    scores = jnp.einsum('btn,bsn->bts', C, B, precision=precise)
    within = jnp.einsum('btsh,bshp->bthp', scores[:, :, :, None] * decays, vals, precision=precise)
    totals = summed[:, -1, :]
    remain = jnp.exp(totals[:, None, :] - summed)
    chunk = jnp.einsum('bsn,bshp->bhnp', B, vals * remain[..., None], precision=precise)
    tc = jnp.cumsum(totals, axis=0)
    tcp = tc - totals
    bi = lax.broadcasted_iota(jnp.int32, (nb, nb), 0)
    bj = lax.broadcasted_iota(jnp.int32, (nb, nb), 1)
    gap = tcp[:, None, :] - tc[None, :, :]
    mprev = jnp.exp(jnp.where((bj < bi)[:, :, None], gap, -1e30))
    start = jnp.einsum('bjh,jhnp->bhnp', mprev, chunk, precision=precise)
    carried = jnp.einsum('btn,bhnp->bthp', C, start, precision=precise) * jnp.exp(summed)[..., None]
    mixed = (within + carried).reshape(R, h, p) + skip_gain[None, :, None] * heads_view
    return mixed.reshape(R, channels)


def gram(left, right):
    return lax.dot_general(
        left, right, (((0,), (0,)), ((), ())), preferred_element_type=jnp.float32
    )


def back_proj(grad_rows, weight):
    return lax.dot_general(
        grad_rows, weight, (((1,), (1,)), ((), ())), preferred_element_type=jnp.float32
    )


def rounded(value):
    return lax.optimization_barrier(value.astype(jnp.bfloat16)).astype(jnp.float32)


def body(
    hidden,
    lengths,
    norm_gain,
    z_weight,
    x_weight,
    bc_weight,
    dt_weight,
    x_kernel,
    bc_kernel,
    x_offset,
    bc_offset,
    step_bias,
    decay_log,
    skip_gain,
    gate_gain,
    out_weight,
    cotangent,
):
    row_count, model_width = hidden.shape
    parts = lax.axis_size("tensor")
    share = row_count // parts
    start = lax.axis_index("tensor") * share
    inputs = hidden.astype(jnp.float32)
    grad_out = cotangent.astype(jnp.float32)
    live_mask = (lax.iota(jnp.int32, row_count) < lengths[0]).astype(jnp.float32)
    scale = lax.rsqrt(jnp.mean(inputs * inputs, axis=1, keepdims=True) + epsilon)
    normed = (inputs * scale * norm_gain[None, :]).astype(jnp.bfloat16)
    gate_pre = jnp.dot(normed, z_weight, preferred_element_type=jnp.float32)
    conv_in = jnp.dot(normed, x_weight, preferred_element_type=jnp.float32)
    state_in = jnp.dot(normed, bc_weight, preferred_element_type=jnp.float32)
    step_raw = jnp.dot(normed, dt_weight, preferred_element_type=jnp.float32)
    conv_out, conv_pull = jax.vjp(conv_act, conv_in, x_kernel, x_offset)
    state_out, state_pull = jax.vjp(conv_act, state_in, bc_kernel, bc_offset)
    conv_low = rounded(conv_out)
    state_low = rounded(state_out)

    def local_mixer(conv_vals, state_vals, raw_steps, bias_steps, decay_logs, skip_gains):
        return mixer(
            conv_vals, state_vals, raw_steps, bias_steps, decay_logs, skip_gains, live_mask
        )

    mixed_out, mixer_pull = jax.vjp(
        local_mixer, conv_low, state_low, step_raw, step_bias, decay_log, skip_gain
    )
    sigmoid_gate = jax.nn.sigmoid(gate_pre)
    silu_gate = gate_pre * sigmoid_gate
    gated = mixed_out * silu_gate
    squares = lax.psum(jnp.sum(gated * gated, axis=1), "tensor")
    inv_norm = lax.rsqrt(squares / DI + epsilon)[:, None]
    unit_rows = gated * inv_norm
    branch_in = (unit_rows * gate_gain[None, :] * live_mask[:, None]).astype(jnp.bfloat16)
    own_inputs = lax.dynamic_slice_in_dim(inputs, start, share, 0)
    own_scale = lax.dynamic_slice_in_dim(scale, start, share, 0)
    branch = lax.psum(jnp.dot(branch_in, out_weight, preferred_element_type=jnp.float32), "tensor")
    output = (inputs + branch).astype(jnp.bfloat16)
    grad_out_weight = gram(branch_in, cotangent)
    grad_branch = back_proj(cotangent, out_weight) * live_mask[:, None]
    grad_gate_gain = jnp.sum(grad_branch * unit_rows, axis=0)
    grad_unit = grad_branch * gate_gain[None, :]
    cross = lax.psum(jnp.sum(grad_unit * unit_rows, axis=1), "tensor")
    grad_gated = inv_norm * (grad_unit - unit_rows * (cross / DI)[:, None])
    grad_mixed = grad_gated * silu_gate
    grad_gate_pre = grad_gated * mixed_out * sigmoid_gate * (1.0 + gate_pre * (1.0 - sigmoid_gate))
    (
        grad_conv_low,
        grad_state_part,
        grad_step_raw,
        grad_step_bias,
        grad_decay_log,
        grad_skip_gain,
    ) = mixer_pull(grad_mixed)
    grad_state_low = lax.psum(grad_state_part, "tensor")
    grad_conv_in, grad_x_kernel, grad_x_offset = conv_pull(grad_conv_low)
    grad_state_in, grad_bc_kernel, grad_bc_offset = state_pull(grad_state_low)
    low_gate = grad_gate_pre.astype(jnp.bfloat16)
    low_conv = grad_conv_in.astype(jnp.bfloat16)
    low_step = grad_step_raw.astype(jnp.bfloat16)
    low_state = lax.dynamic_slice_in_dim(grad_state_in, start, share, 0).astype(jnp.bfloat16)
    own_normed = lax.dynamic_slice_in_dim(normed, start, share, 0)
    grad_z_weight = gram(normed, low_gate)
    grad_x_weight = gram(normed, low_conv)
    grad_dt_weight = gram(normed, low_step)
    grad_bc_weight = gram(own_normed, low_state)
    state_back = back_proj(low_state, bc_weight)
    grad_normed = (
        back_proj(low_gate, z_weight)
        + back_proj(low_conv, x_weight)
        + back_proj(low_step, dt_weight)
    )
    own_part = lax.dynamic_slice_in_dim(grad_normed, start, share, 0) + state_back
    grad_normed = lax.dynamic_update_slice_in_dim(grad_normed, own_part, start, 0)
    grad_normed = lax.psum(grad_normed, "tensor")
    weighted = grad_normed * norm_gain[None, :]
    row_dots = jnp.sum(weighted * inputs, axis=1, keepdims=True)
    grad_hidden = (
        grad_out + scale * weighted - inputs * scale * scale * scale * row_dots / model_width
    )
    own_grad = lax.dynamic_slice_in_dim(grad_normed, start, share, 0)
    grad_norm_gain = jnp.sum(own_grad * own_inputs * own_scale, axis=0)
    (
        grad_z_weight,
        grad_x_weight,
        grad_dt_weight,
        grad_out_weight,
        grad_x_kernel,
        grad_x_offset,
        grad_step_bias,
        grad_decay_log,
        grad_skip_gain,
        grad_gate_gain,
        grad_bc_kernel,
        grad_bc_offset,
    ) = lax.psum(
        (
            grad_z_weight,
            grad_x_weight,
            grad_dt_weight,
            grad_out_weight,
            grad_x_kernel,
            grad_x_offset,
            grad_step_bias,
            grad_decay_log,
            grad_skip_gain,
            grad_gate_gain,
            grad_bc_kernel,
            grad_bc_offset,
        ),
        "dp",
    )
    grad_bc_weight, grad_norm_gain = lax.psum((grad_bc_weight, grad_norm_gain), ("dp", "tensor"))
    return (
        output,
        grad_hidden,
        grad_norm_gain,
        grad_z_weight,
        grad_x_weight,
        grad_bc_weight,
        grad_dt_weight,
        grad_x_kernel,
        grad_bc_kernel,
        grad_x_offset,
        grad_bc_offset,
        grad_step_bias,
        grad_decay_log,
        grad_skip_gain,
        grad_gate_gain,
        grad_out_weight,
    )


def solution(mesh):
    placed = (
        P("dp", None),
        P("dp"),
        P(),
        P(None, "tensor"),
        P(None, "tensor"),
        P(),
        P(None, "tensor"),
        P(None, "tensor"),
        P(),
        P("tensor"),
        P(),
        P("tensor"),
        P("tensor"),
        P("tensor"),
        P("tensor"),
        P("tensor", None),
        P("dp", None),
    )
    return jax.shard_map(
        body,
        mesh=mesh,
        in_specs=placed,
        out_specs=(
            P("dp", None),
            P("dp", None),
            P(),
            P(None, "tensor"),
            P(None, "tensor"),
            P(),
            P(None, "tensor"),
            P(None, "tensor"),
            P(),
            P("tensor"),
            P(),
            P("tensor"),
            P("tensor"),
            P("tensor"),
            P("tensor"),
            P("tensor", None),
        ),
        check_vma=False,
    )
```
